256 devices in a mesh: dp: 8 (over z), seq: 32 (over y, x, core).
Axes of the slice: x: 4, y: 4, z: 8, core: 2. Of those that a mesh axis runs over, the one named last changes fastest.
Arguments:
- tokens: int32 [8, 16384], P('dp', 'seq'), may hold values from 0 to 3
- embed_table: bfloat16 [4, 768], replicated, may hold values from -6 to 6
- mix_weight: bfloat16 [2, 768, 768], replicated, may hold values from -0.21875 to 0.21875
- kernels: bfloat16 [2, 3, 768], replicated, may hold values from -3.5 to 3.5
- donor_proj: bfloat16 [768, 256], replicated, may hold values from -0.21875 to 0.21875
- acceptor_proj: bfloat16 [768, 256], replicated, may hold values from -0.21875 to 0.21875
- tissue_scale: float32 [4, 256], replicated, may hold values from -0.375 to 0.375
- junction_dest: int32 [8, 8192, 1], P('dp', 'seq'), may hold values from 0 to 31; in each aligned block of 256 rows (0 to 255, 256 to 511, ..., all dimensions but the last counted through in order) at most 16 rows name the same one
- donor_offset: int32 [8, 8192], P('dp', 'seq'), may hold values from 0 to 511
- acceptor_offset: int32 [8, 8192], P('dp', 'seq'), may hold values from 0 to 511
- tissue_ids: int32 [8, 8192], P('dp', 'seq'), may hold values from 0 to 3
- targets: float32 [8, 8192], P('dp', 'seq'), may hold values from -6 to 6
Outputs:
- features: bfloat16 [8, 16384, 768], P('dp', 'seq')
- input_grad: bfloat16 [8, 16384, 768], P('dp', 'seq')
- mix_grad: float32 [2, 768, 768], P(None, 'dp')
- kernel_grad: float32 [2, 3, 768], P(None, None, 'dp')
- embed_grad: float32 [4, 768], P(None, 'dp')
- donor_grad: float32 [768, 256], P('dp')
- acceptor_grad: float32 [768, 256], P('dp')
- tissue_grad: float32 [4, 256], P(None, 'dp')
The draws below stay inside these ranges and needn't reach their ends.
Inputs may be any that keep to these rules, and one draw needn't show every extreme that they name: `junction_dest`: in each aligned block of 256 rows (the junctions of one device) no value appears more than 16 times, a bound that some block reaches.
All inputs are finite; a program needn't handle non-finite values.
Results may differ from the reference program's by a relative error of at most 0.02.
Values may be sent and summed in bfloat16 or wider, within the bound.
No kernel may reach another device: no remote copies, remote signals or barrier semaphores. Data moves between devices by JAX's collectives and lax.ppermute only.
A program may use at most 64 MiB of HBM per device.

```python
import math
import jax
import jax.numpy as jnp
import numpy as np
from jax import lax

C = 768
E = 256
TISSUES = 4
FIRST_DILATION = 16
SECOND_DILATION = 128
L_DEV = 512
JUNC_DEV = 256
SEQLEN = 16384
EXAMPLES = 8
JUNCS = 8192
CAP = 16
N_SEQ = 32


def set_ends(entries, key, smallest, high):
    longest = entries.shape.index(max(entries.shape))
    spots = []
    for shift in (0, 1):
        where = [jax.random.randint(jax.random.fold_in(key, axis), (), 0, length) for axis, length in enumerate(entries.shape)]
        where[longest] = (where[longest] + shift) % entries.shape[longest]
        spots.append(tuple(where))
    return entries.at[spots[0]].set(smallest).at[spots[1]].set(high)


def level_of(rng, shape, split, least, largest):
    def one(axis_at, parts):
        draws = jax.random.uniform(jax.random.fold_in(jax.random.fold_in(rng, 6), axis_at), (parts,), jnp.float32, least / len(split), largest / len(split))
        return jnp.repeat(jnp.exp(draws), shape[axis_at] // parts).reshape((-1,) + (1,) * (len(shape) - axis_at - 1))

    factor_of = one(*split[0])
    for cut in split[1:]:
        factor_of = factor_of * one(*cut)
    return factor_of


def routed_block(key, own, number, rows, amount, top, reach, skew):
    ranking = jax.random.permutation(key, amount)
    heavy_load, common = shares(amount, rows * top, reach, skew, True), shares(amount, rows * top, reach, skew, False)
    places = jnp.arange(amount)

    def named(lengths, offset_by):
        used = int((lengths > 0).sum())
        fixed = max(1, used // 4)
        passed = fixed + (places - fixed + offset_by * (used - fixed)) % max(1, amount - fixed)
        return jnp.zeros((amount,), jnp.int32).at[ranking[jnp.where(places < fixed, places, passed)]].set(jnp.asarray(lengths, jnp.int32))

    lengths = jnp.where(number % 4 == 0, named(heavy_load, number // 4), named(common, number - number // 4 - 1))
    mixed = jax.random.permutation(jax.random.fold_in(own, 3), amount)
    giver, taker = mixed[0:amount // 2 * 2:2], mixed[1:amount // 2 * 2:2]
    margin = jnp.minimum(lengths[giver] - 1, reach - lengths[taker]) // 2
    margin = jnp.where((giver == ranking[0]) | (taker == ranking[0]) | (lengths[taker] == 0), 0, jnp.maximum(margin, 0))
    passed = jax.random.randint(jax.random.fold_in(own, 4), (amount // 2,), 0, 1 << 20) % (margin + 1)
    lengths = lengths.at[giver].add(-passed).at[taker].add(passed)
    members = jnp.searchsorted(jnp.cumsum(lengths), jnp.arange(rows * top), side="right").astype(jnp.int32)
    listing = members.reshape(top, rows).T
    listing = listing[jax.random.permutation(jax.random.fold_in(own, 1), rows)]
    offset_by = jax.random.randint(jax.random.fold_in(own, 2), (rows, 1), 0, top)
    return jnp.take_along_axis(listing, (jnp.arange(top)[None, :] + offset_by) % top, axis=1)


def shares(amount, total, bound, skew, full):
    loads = [(1 << 20) // math.isqrt(rank ** skew) + 1 for rank in range(1, amount + 1)]
    largest = bound if full else min(bound, max(-(-total // amount), total * loads[0] // sum(loads)))
    least = 1 if total - largest >= amount - 1 else 0
    holding, spare = [largest] + [least] * (amount - 1), total - largest - least * (amount - 1)
    while spare > 0:
        movable = [i for i in range(1, amount) if holding[i] < largest] or [i for i in range(1, amount) if holding[i] < bound]
        mass, budget = sum([loads[i] for i in movable]), spare
        for i in movable:
            addition = min(bound - holding[i], max(1, budget * loads[i] // mass), spare)
            holding[i] = holding[i] + addition
            spare = spare - addition
    return np.array(holding)


def scatter_about(own_key, extent, deviation, limit, split=(), kind=jnp.bfloat16):
    level = level_of(own_key, extent, split, -0.22, 0.18) if split else 1.0
    drawn = jax.random.normal(own_key, extent, jnp.float32) * deviation * level
    return jnp.minimum(jnp.maximum(drawn, -limit), limit).astype(kind)


def setup_inputs(seed: int = 0) -> dict:
    splits = jax.random.split(jax.random.key(seed), 13)
    tokens = set_ends(jax.random.randint(splits[0], (EXAMPLES, SEQLEN), 0, 4), jax.random.fold_in(splits[0], 1), 0, 3).astype(jnp.int32)
    embed_table = scatter_about(splits[1], (4, C), 1.0, 6.0)
    mix_weight = scatter_about(splits[2], (2, C, C), C ** -0.5, 0.21875)
    kernels = scatter_about(splits[3], (2, 3, C), 3 ** -0.5, 3.5)
    donor_proj = scatter_about(splits[4], (C, E), C ** -0.5, 0.21875)
    acceptor_proj = scatter_about(splits[5], (C, E), C ** -0.5, 0.21875)
    tissue_scale = scatter_about(splits[6], (TISSUES, E), E ** -0.5, 0.375, (), jnp.float32)
    junction_dest_keys = jax.random.split(jax.random.fold_in(splits[7], 1), EXAMPLES * JUNCS // JUNC_DEV)
    junction_dest_turns = jax.random.permutation(jax.random.fold_in(splits[7], 3), EXAMPLES * JUNCS // JUNC_DEV)
    junction_dest = jax.vmap(lambda own, number: routed_block(jax.random.fold_in(splits[7], 2), own, number, JUNC_DEV, N_SEQ, 1, CAP, 2))(junction_dest_keys, junction_dest_turns).reshape((EXAMPLES, JUNCS, 1))
    donor_offset = set_ends(jax.random.randint(splits[8], (EXAMPLES, JUNCS), 0, L_DEV), jax.random.fold_in(splits[8], 1), 0, L_DEV - 1).astype(jnp.int32)
    acceptor_offset = set_ends(jax.random.randint(splits[9], (EXAMPLES, JUNCS), 0, L_DEV), jax.random.fold_in(splits[9], 1), 0, L_DEV - 1).astype(jnp.int32)
    tissue_ids = set_ends(jax.random.randint(splits[10], (EXAMPLES, JUNCS), 0, TISSUES), jax.random.fold_in(splits[10], 1), 0, TISSUES - 1).astype(jnp.int32)
    targets = scatter_about(splits[11], (EXAMPLES, JUNCS), 1.0, 6.0, ((0, 8), (1, 32)), jnp.float32)
    return {"tokens": tokens, "embed_table": embed_table, "mix_weight": mix_weight, "kernels": kernels, "donor_proj": donor_proj, "acceptor_proj": acceptor_proj, "tissue_scale": tissue_scale, "junction_dest": junction_dest, "donor_offset": donor_offset, "acceptor_offset": acceptor_offset, "tissue_ids": tissue_ids, "targets": targets}


epsilon = 1e-06

def normalize(stream_wide):
    inv_rms = lax.rsqrt(lax.optimization_barrier(jnp.mean(stream_wide * stream_wide, axis=-1, keepdims=True)) + epsilon)
    return (stream_wide * inv_rms, inv_rms)

def offset_rows(values, distance):
    count = values.shape[0]
    zeros = jnp.zeros((abs(distance),) + values.shape[1:], values.dtype)
    if distance > 0:
        return jnp.concatenate([values[distance:], zeros], 0)
    return jnp.concatenate([zeros, values[:count + distance]], 0)

def gelu_tanh(values):
    return jax.nn.gelu(values, approximate=True)

def reference(tokens, embed_table, mix_weight, kernels, donor_proj, acceptor_proj, tissue_scale, junction_dest, donor_offset, acceptor_offset, tissue_ids, targets):
    dilation_sizes = (FIRST_DILATION, SECOND_DILATION)
    mix_acc = [jnp.zeros((C, C), jnp.float32), jnp.zeros((C, C), jnp.float32)]
    kernel_acc = [jnp.zeros((3, C), jnp.float32), jnp.zeros((3, C), jnp.float32)]
    embed_acc = jnp.zeros((4, C), jnp.float32)
    tissue_acc = jnp.zeros((TISSUES, E), jnp.float32)
    donor_acc = jnp.zeros((C, E), jnp.float32)
    acceptor_accumulator = jnp.zeros((C, E), jnp.float32)
    feature_list = []
    grad_list = []
    for example in range(EXAMPLES):
        tok_row = tokens[example]
        stream = embed_table[tok_row]
        saved = []
        for layer_index in range(2):
            dilation = dilation_sizes[layer_index]
            stream_wide = stream.astype(jnp.float32)
            normed, inv_rms = normalize(stream_wide)
            norm_wide = normed.astype(jnp.bfloat16).astype(jnp.float32)
            kernel_wide = kernels[layer_index].astype(jnp.float32)
            conv_out = kernel_wide[0] * offset_rows(norm_wide, -dilation) + kernel_wide[1] * norm_wide + kernel_wide[2] * offset_rows(norm_wide, dilation)
            activated = gelu_tanh(conv_out).astype(jnp.bfloat16)
            updated_params = stream_wide + jnp.dot(activated, mix_weight[layer_index], preferred_element_type=jnp.float32)
            saved.append((normed, inv_rms, norm_wide, conv_out, activated))
            stream = updated_params.astype(jnp.bfloat16)
        feature_list.append(stream)
        junction_index = jnp.arange(JUNCS, dtype=jnp.int32)
        donor_pos = junction_index // JUNC_DEV * L_DEV + donor_offset[example]
        accept_pos = junction_dest[example, :, 0] * L_DEV + acceptor_offset[example]
        donors = stream[donor_pos]
        accepted = stream[accept_pos]
        donor_emb = jnp.dot(donors, donor_proj, preferred_element_type=jnp.float32)
        accept_emb = jnp.dot(accepted, acceptor_proj, preferred_element_type=jnp.float32).astype(jnp.bfloat16).astype(jnp.float32)
        tissue_rows = tissue_scale[tissue_ids[example]]
        score = lax.optimization_barrier(jnp.sum(donor_emb * accept_emb * tissue_rows, axis=-1))
        misfit = score - targets[example]
        donor_back = (misfit[:, None] * accept_emb * tissue_rows).astype(jnp.bfloat16)
        accept_back = (misfit[:, None] * donor_emb * tissue_rows).astype(jnp.bfloat16)
        tissue_acc = tissue_acc + jax.ops.segment_sum(misfit[:, None] * donor_emb * accept_emb, tissue_ids[example], num_segments=TISSUES)
        donor_acc = donor_acc + jnp.dot(donors.T, donor_back, preferred_element_type=jnp.float32)
        acceptor_accumulator = acceptor_accumulator + jnp.dot(accepted.T, accept_back, preferred_element_type=jnp.float32)
        upstream = jnp.zeros((SEQLEN, C), jnp.float32)
        upstream = upstream.at[donor_pos].add(jnp.dot(donor_back, donor_proj.T, preferred_element_type=jnp.float32))
        upstream = upstream.at[accept_pos].add(jnp.dot(accept_back, acceptor_proj.T, preferred_element_type=jnp.float32))
        for layer_index in (1, 0):
            dilation = dilation_sizes[layer_index]
            normed, inv_rms, norm_wide, conv_out, activated = saved[layer_index]
            upstream_low = upstream.astype(jnp.bfloat16)
            mix_acc[layer_index] = mix_acc[layer_index] + jnp.dot(activated.T, upstream_low, preferred_element_type=jnp.float32)
            act_grad = jnp.dot(upstream_low, mix_weight[layer_index].T, preferred_element_type=jnp.float32)
            gelu_value, pullback = jax.vjp(gelu_tanh, conv_out)
            conv_wide = pullback(act_grad)[0].astype(jnp.bfloat16).astype(jnp.float32)
            kernel_rows = jnp.stack([lax.optimization_barrier(jnp.sum(conv_wide * offset_rows(norm_wide, -dilation), axis=0)), lax.optimization_barrier(jnp.sum(conv_wide * norm_wide, axis=0)), lax.optimization_barrier(jnp.sum(conv_wide * offset_rows(norm_wide, dilation), axis=0))])
            kernel_acc[layer_index] = kernel_acc[layer_index] + kernel_rows
            kernel_wide = kernels[layer_index].astype(jnp.float32)
            norm_grad = kernel_wide[0] * offset_rows(conv_wide, dilation) + kernel_wide[1] * conv_wide + kernel_wide[2] * offset_rows(conv_wide, -dilation)
            upstream = upstream + inv_rms * (norm_grad - normed * lax.optimization_barrier(jnp.mean(norm_grad * normed, axis=-1, keepdims=True)))
        grad_list.append(upstream.astype(jnp.bfloat16))
        embed_acc = embed_acc + jax.ops.segment_sum(upstream, tok_row, num_segments=4)
    features = jnp.stack(feature_list)
    input_grad = jnp.stack(grad_list)
    return (features, input_grad, jnp.stack(mix_acc), jnp.stack(kernel_acc), embed_acc, donor_acc, acceptor_accumulator, tissue_acc)
```

```python
import jax
import jax.numpy as jnp
from jax import lax
from jax.sharding import PartitionSpec as P

FIRST_DILATION = 16
SECOND_DILATION = 128


epsilon = 1e-06


def padded(cells, sides, width):
    for axis, dim in sides:
        count = lax.axis_size(axis)
        ends = count - 1
        head = lax.slice_in_dim(cells, 0, width, axis=dim)
        tail = lax.slice_in_dim(cells, cells.shape[dim] - width, cells.shape[dim], axis=dim)
        cells = jnp.concatenate(
            [
                lax.ppermute(tail, axis, [(i, (i + 1) % count) for i in range(ends)]),
                cells,
                lax.ppermute(head, axis, [((i + 1) % count, i) for i in range(ends)]),
            ],
            axis=dim,
        )
    return cells


def normalize(stream_wide):
    inv_rms = lax.rsqrt(jnp.mean(stream_wide * stream_wide, axis=-1, keepdims=True) + epsilon)
    return (stream_wide * inv_rms, inv_rms)


def gelu_tanh(values):
    return jax.nn.gelu(values, approximate=True)


def norm_halo(norm_low, dilation):
    return padded(norm_low, (("seq", 0),), dilation)


def grad_halo(conv_low, dilation):
    return padded(conv_low, (("seq", 0),), dilation)


def per_device(
    tokens,
    embed_table,
    mix_weight,
    kernels,
    donor_proj,
    acceptor_proj,
    tissue_scale,
    junction_dest,
    donor_offset,
    acceptor_offset,
    tissue_ids,
    targets,
):
    length = tokens.shape[1]
    tok_row = tokens[0]
    vocab_hits = tok_row[:, None] == jnp.arange(embed_table.shape[0], dtype=jnp.int32)[None, :]
    stream = jnp.dot(
        vocab_hits.astype(jnp.bfloat16), embed_table, preferred_element_type=jnp.float32
    ).astype(jnp.bfloat16)
    dilation_sizes = (FIRST_DILATION, SECOND_DILATION)
    saved = []
    for layer_index in range(2):
        dilation = dilation_sizes[layer_index]
        stream_wide = stream.astype(jnp.float32)
        normed, inv_rms = normalize(stream_wide)
        norm_low = normed.astype(jnp.bfloat16)
        padded_input = norm_halo(norm_low, dilation)
        padded_wide = padded_input.astype(jnp.float32)
        kernel_wide = kernels[layer_index].astype(jnp.float32)
        conv_out = (
            kernel_wide[0] * padded_wide[:length]
            + kernel_wide[1] * padded_wide[dilation : dilation + length]
            + kernel_wide[2] * padded_wide[2 * dilation :]
        )
        activated = gelu_tanh(conv_out).astype(jnp.bfloat16)
        updated_params = stream_wide + jnp.dot(
            activated, mix_weight[layer_index], preferred_element_type=jnp.float32
        )
        saved.append((normed, inv_rms, padded_input, conv_out, activated))
        stream = updated_params.astype(jnp.bfloat16)
    dest = junction_dest[0, :, 0]
    donor_rows = donor_offset[0]
    accept_rows = acceptor_offset[0]
    tissue_row = tissue_ids[0]
    count = lax.axis_size("seq")
    capacity = 2 * dest.shape[0] // count
    dest_hits = (dest[:, None] == jnp.arange(count, dtype=jnp.int32)[None, :]).astype(jnp.int32)
    before = jnp.cumsum(dest_hits, axis=0) - dest_hits
    slot = jnp.sum(before * dest_hits, axis=1)
    key = dest * capacity + slot
    key_hits = key[:, None] == jnp.arange(count * capacity, dtype=jnp.int32)[None, :]
    request = (
        jnp.sum(jnp.where(key_hits, accept_rows[:, None] + 1, 0), axis=0) - 1
    ).reshape(count, capacity)
    asked = lax.all_to_all(request, "seq", split_axis=0, concat_axis=0, tiled=True)
    valid = (asked >= 0).reshape(-1)
    asked_rows = jnp.where(valid, asked.reshape(-1), 0)
    accepted = stream[asked_rows]
    accept_emb = jnp.dot(accepted, acceptor_proj, preferred_element_type=jnp.float32)
    answer = (
        jnp.where(valid[:, None], accept_emb, 0.0).astype(jnp.bfloat16).reshape(count, capacity, -1)
    )
    returned = lax.all_to_all(answer, "seq", split_axis=0, concat_axis=0, tiled=True)
    key_low = key_hits.astype(jnp.bfloat16)
    accept_wide = jnp.dot(
        key_low, returned.reshape(count * capacity, -1), preferred_element_type=jnp.float32
    )
    donors = stream[donor_rows]
    donor_emb = jnp.dot(donors, donor_proj, preferred_element_type=jnp.float32)
    tissue_hits = (
        tissue_row[:, None] == jnp.arange(tissue_scale.shape[0], dtype=jnp.int32)[None, :]
    ).astype(jnp.float32)
    tissue_rows = jnp.dot(tissue_hits, tissue_scale, precision=lax.Precision.HIGHEST)
    score = jnp.sum(donor_emb * accept_wide * tissue_rows, axis=-1)
    misfit = score - targets[0]
    donor_back = (misfit[:, None] * accept_wide * tissue_rows).astype(jnp.bfloat16)
    accept_back = (misfit[:, None] * donor_emb * tissue_rows).astype(jnp.bfloat16)
    tissue_part = jnp.dot(
        tissue_hits.T, misfit[:, None] * donor_emb * accept_wide, precision=lax.Precision.HIGHEST
    )
    donor_part = jnp.dot(donors.T, donor_back, preferred_element_type=jnp.float32)
    back_buffer = (
        jnp.dot(key_low.T, accept_back, preferred_element_type=jnp.float32)
        .astype(jnp.bfloat16)
        .reshape(count, capacity, -1)
    )
    accept_grads = lax.all_to_all(
        back_buffer, "seq", split_axis=0, concat_axis=0, tiled=True
    ).reshape(count * capacity, -1)
    accept_part = jnp.dot(accepted.T, accept_grads, preferred_element_type=jnp.float32)
    positions = jnp.arange(length, dtype=jnp.int32)[None, :]
    donor_hits = (donor_rows[:, None] == positions).astype(jnp.float32)
    asked_hits = ((asked_rows[:, None] == positions) & valid[:, None]).astype(jnp.float32)
    upstream = jnp.dot(
        donor_hits.T,
        jnp.dot(donor_back, donor_proj.T, preferred_element_type=jnp.float32),
        precision=lax.Precision.HIGHEST,
    ) + jnp.dot(
        asked_hits.T,
        jnp.dot(accept_grads, acceptor_proj.T, preferred_element_type=jnp.float32),
        precision=lax.Precision.HIGHEST,
    )
    mix_parts = [None, None]
    kernel_parts = [None, None]
    for layer_index in (1, 0):
        dilation = dilation_sizes[layer_index]
        normed, inv_rms, stored, conv_out, activated = saved[layer_index]
        upstream_low = upstream.astype(jnp.bfloat16)
        mix_parts[layer_index] = jnp.dot(
            activated.T, upstream_low, preferred_element_type=jnp.float32
        )
        act_grad = jnp.dot(
            upstream_low, mix_weight[layer_index].T, preferred_element_type=jnp.float32
        )
        gelu_value, pullback = jax.vjp(gelu_tanh, conv_out)
        conv_low = pullback(act_grad)[0].astype(jnp.bfloat16)
        padded_wide = stored.astype(jnp.float32)
        grad_padded = grad_halo(conv_low, dilation).astype(jnp.float32)
        conv_wide = grad_padded[dilation : dilation + length]
        kernel_parts[layer_index] = jnp.stack(
            [
                jnp.sum(conv_wide * padded_wide[:length], axis=0),
                jnp.sum(conv_wide * padded_wide[dilation : dilation + length], axis=0),
                jnp.sum(conv_wide * padded_wide[2 * dilation :], axis=0),
            ]
        )
        kernel_wide = kernels[layer_index].astype(jnp.float32)
        norm_grad = (
            kernel_wide[0] * grad_padded[2 * dilation :]
            + kernel_wide[1] * conv_wide
            + kernel_wide[2] * grad_padded[:length]
        )
        upstream = upstream + inv_rms * (
            norm_grad - normed * jnp.mean(norm_grad * normed, axis=-1, keepdims=True)
        )
    embed_part = jnp.dot(
        vocab_hits.astype(jnp.float32).T, upstream, precision=lax.Precision.HIGHEST
    )
    groups = lax.axis_size("dp")
    channels = stream.shape[1]
    tissues, width = tissue_part.shape
    rows = channels // groups
    lanes = 128
    tissue_cells = (
        tissue_part.reshape(tissues, groups, width // groups)
        .transpose(1, 0, 2)
        .reshape(groups, -1)
    )
    tissue_cols = -(-tissue_cells.shape[1] // rows)
    tissue_cells = jnp.pad(
        tissue_cells, ((0, 0), (0, tissue_cols * rows - tissue_cells.shape[1]))
    ).reshape(channels, tissue_cols)
    kernel_local = jnp.stack(kernel_parts).reshape(-1, channels).T
    small = jnp.concatenate([kernel_local, embed_part.T, tissue_cells], axis=1)
    small_widths = [kernel_local.shape[1], embed_part.shape[0], tissue_cols]
    big = [mix_parts[0], mix_parts[1], donor_part, accept_part]
    big_total = sum(piece.shape[1] for piece in big)
    total = -(-(big_total + small.shape[1]) // (2 * lanes)) * (2 * lanes)
    packed = jnp.concatenate(
        [piece.astype(jnp.bfloat16) for piece in big]
        + [
            jnp.pad(small, ((0, 0), (0, total - big_total - small.shape[1]))).astype(
                jnp.bfloat16
            )
        ],
        axis=1,
    )
    half = total // 2
    core = lax.axis_index("seq") % 2
    own = lax.dynamic_slice_in_dim(packed, core * half, half, axis=1)
    other = lax.dynamic_slice_in_dim(packed, (1 - core) * half, half, axis=1)
    partner = lax.ppermute(other, "seq", [(i, i ^ 1) for i in range(count)])
    pair_sum = (own.astype(jnp.float32) + partner.astype(jnp.float32)).astype(jnp.bfloat16)
    scattered = lax.psum_scatter(pair_sum, "dp", scatter_dimension=0, tiled=True)
    share = rows // count
    blocks = scattered.reshape(count, share * half)
    exchanged = lax.all_to_all(blocks, "seq", split_axis=0, concat_axis=0, tiled=True)
    by_core = exchanged.astype(jnp.float32).reshape(count // 2, 2, share * half)
    own_sum = jnp.sum(by_core, axis=0).astype(jnp.bfloat16)
    gathered = lax.all_gather(own_sum, "seq", axis=0, tiled=False)
    summed = jnp.concatenate(
        [gathered[:, 0].reshape(rows, half), gathered[:, 1].reshape(rows, half)], axis=1
    ).astype(jnp.float32)
    mix_grad = summed[:, : 2 * channels].reshape(rows, 2, channels).transpose(1, 0, 2)
    proj_width = donor_part.shape[1]
    donor_grad = summed[:, 2 * channels : 2 * channels + proj_width]
    accept_grad = summed[:, 2 * channels + proj_width : big_total]
    k0 = big_total
    k1 = k0 + small_widths[0]
    k2 = k1 + small_widths[1]
    k3 = k2 + small_widths[2]
    kernel_grad = summed[:, k0:k1].T.reshape(2, 3, rows)
    embed_grad = summed[:, k1:k2].T
    tissue_grad = (
        summed[:, k2:k3].reshape(-1)[: tissues * (width // groups)].reshape(tissues, width // groups)
    )
    features = stream[None]
    input_grad = upstream.astype(jnp.bfloat16)[None]
    return (
        features,
        input_grad,
        mix_grad,
        kernel_grad,
        embed_grad,
        donor_grad,
        accept_grad,
        tissue_grad,
    )


def solution(mesh):
    placed = (
        P("dp", "seq"),
        P(),
        P(),
        P(),
        P(),
        P(),
        P(),
        P("dp", "seq", None),
        P("dp", "seq"),
        P("dp", "seq"),
        P("dp", "seq"),
        P("dp", "seq"),
    )
    return jax.shard_map(
        per_device,
        mesh=mesh,
        in_specs=placed,
        out_specs=(
            P("dp", "seq", None),
            P("dp", "seq", None),
            P(None, "dp", None),
            P(None, None, "dp"),
            P(None, "dp"),
            P("dp", None),
            P("dp", None),
            P(None, "dp"),
        ),
        check_vma=False,
    )
```

```python
import jax
import jax.numpy as jnp
from jax import lax
from jax.sharding import PartitionSpec as P

FIRST_DILATION = 16
SECOND_DILATION = 128


epsilon = 1e-06


def padded(cells, sides, width):
    for axis, dim in sides:
        count = lax.axis_size(axis)
        ends = count - 1
        head = lax.slice_in_dim(cells, 0, width, axis=dim)
        tail = lax.slice_in_dim(cells, cells.shape[dim] - width, cells.shape[dim], axis=dim)
        cells = jnp.concatenate(
            [
                lax.ppermute(tail, axis, [(i, (i + 1) % count) for i in range(ends)]),
                cells,
                lax.ppermute(head, axis, [((i + 1) % count, i) for i in range(ends)]),
            ],
            axis=dim,
        )
    return cells


def normalize(stream_wide):
    inv_rms = lax.rsqrt(jnp.mean(stream_wide * stream_wide, axis=-1, keepdims=True) + epsilon)
    return (stream_wide * inv_rms, inv_rms)


def gelu_tanh(values):
    return jax.nn.gelu(values, approximate=True)


def norm_halo(norm_low, dilation):
    return padded(norm_low, (("seq", 0),), dilation)


def grad_halo(conv_low, dilation):
    return padded(conv_low, (("seq", 0),), dilation)


def per_device(
    tokens,
    embed_table,
    mix_weight,
    kernels,
    donor_proj,
    acceptor_proj,
    tissue_scale,
    junction_dest,
    donor_offset,
    acceptor_offset,
    tissue_ids,
    targets,
):
    length = tokens.shape[1]
    tok_row = tokens[0]
    vocab_hits = tok_row[:, None] == jnp.arange(embed_table.shape[0], dtype=jnp.int32)[None, :]
    stream = jnp.dot(
        vocab_hits.astype(jnp.bfloat16), embed_table, preferred_element_type=jnp.float32
    ).astype(jnp.bfloat16)
    dilation_sizes = (FIRST_DILATION, SECOND_DILATION)
    saved = []
    for layer_index in range(2):
        dilation = dilation_sizes[layer_index]
        stream_wide = stream.astype(jnp.float32)
        normed, inv_rms = normalize(stream_wide)
        norm_low = normed.astype(jnp.bfloat16)
        padded_input = norm_halo(norm_low, dilation)
        padded_wide = padded_input.astype(jnp.float32)
        kernel_wide = kernels[layer_index].astype(jnp.float32)
        conv_out = (
            kernel_wide[0] * padded_wide[:length]
            + kernel_wide[1] * padded_wide[dilation : dilation + length]
            + kernel_wide[2] * padded_wide[2 * dilation :]
        )
        activated = gelu_tanh(conv_out).astype(jnp.bfloat16)
        updated_params = stream_wide + jnp.dot(
            activated, mix_weight[layer_index], preferred_element_type=jnp.float32
        )
        saved.append((normed, inv_rms, padded_input, conv_out, activated))
        stream = updated_params.astype(jnp.bfloat16)
    dest = junction_dest[0, :, 0]
    donor_rows = donor_offset[0]
    accept_rows = acceptor_offset[0]
    tissue_row = tissue_ids[0]
    count = lax.axis_size("seq")
    capacity = 2 * dest.shape[0] // count
    dest_hits = (dest[:, None] == jnp.arange(count, dtype=jnp.int32)[None, :]).astype(jnp.int32)
    before = jnp.cumsum(dest_hits, axis=0) - dest_hits
    slot = jnp.sum(before * dest_hits, axis=1)
    key = dest * capacity + slot
    key_hits = key[:, None] == jnp.arange(count * capacity, dtype=jnp.int32)[None, :]
    request = (
        jnp.sum(jnp.where(key_hits, accept_rows[:, None] + 1, 0), axis=0) - 1
    ).reshape(count, capacity)
    asked = lax.all_to_all(request, "seq", split_axis=0, concat_axis=0, tiled=True)
    valid = (asked >= 0).reshape(-1)
    asked_rows = jnp.where(valid, asked.reshape(-1), 0)
    accepted = stream[asked_rows]
    accept_emb = jnp.dot(accepted, acceptor_proj, preferred_element_type=jnp.float32)
    answer = (
        jnp.where(valid[:, None], accept_emb, 0.0).astype(jnp.bfloat16).reshape(count, capacity, -1)
    )
    returned = lax.all_to_all(answer, "seq", split_axis=0, concat_axis=0, tiled=True)
    key_low = key_hits.astype(jnp.bfloat16)
    accept_wide = jnp.dot(
        key_low, returned.reshape(count * capacity, -1), preferred_element_type=jnp.float32
    )
    donors = stream[donor_rows]
    donor_emb = jnp.dot(donors, donor_proj, preferred_element_type=jnp.float32)
    tissue_hits = (
        tissue_row[:, None] == jnp.arange(tissue_scale.shape[0], dtype=jnp.int32)[None, :]
    ).astype(jnp.float32)
    tissue_rows = jnp.dot(tissue_hits, tissue_scale, precision=lax.Precision.HIGHEST)
    score = jnp.sum(donor_emb * accept_wide * tissue_rows, axis=-1)
    misfit = score - targets[0]
    donor_back = (misfit[:, None] * accept_wide * tissue_rows).astype(jnp.bfloat16)
    accept_back = (misfit[:, None] * donor_emb * tissue_rows).astype(jnp.bfloat16)
    tissue_part = jnp.dot(
        tissue_hits.T, misfit[:, None] * donor_emb * accept_wide, precision=lax.Precision.HIGHEST
    )
    donor_part = jnp.dot(donors.T, donor_back, preferred_element_type=jnp.float32)
    back_buffer = (
        jnp.dot(key_low.T, accept_back, preferred_element_type=jnp.float32)
        .astype(jnp.bfloat16)
        .reshape(count, capacity, -1)
    )
    accept_grads = lax.all_to_all(
        back_buffer, "seq", split_axis=0, concat_axis=0, tiled=True
    ).reshape(count * capacity, -1)
    accept_part = jnp.dot(accepted.T, accept_grads, preferred_element_type=jnp.float32)
    positions = jnp.arange(length, dtype=jnp.int32)[None, :]
    donor_hits = (donor_rows[:, None] == positions).astype(jnp.float32)
    asked_hits = ((asked_rows[:, None] == positions) & valid[:, None]).astype(jnp.float32)
    upstream = jnp.dot(
        donor_hits.T,
        jnp.dot(donor_back, donor_proj.T, preferred_element_type=jnp.float32),
        precision=lax.Precision.HIGHEST,
    ) + jnp.dot(
        asked_hits.T,
        jnp.dot(accept_grads, acceptor_proj.T, preferred_element_type=jnp.float32),
        precision=lax.Precision.HIGHEST,
    )
    mix_parts = [None, None]
    kernel_parts = [None, None]
    for layer_index in (1, 0):
        dilation = dilation_sizes[layer_index]
        normed, inv_rms, stored, conv_out, activated = saved[layer_index]
        upstream_low = upstream.astype(jnp.bfloat16)
        mix_parts[layer_index] = jnp.dot(
            activated.T, upstream_low, preferred_element_type=jnp.float32
        )
        act_grad = jnp.dot(
            upstream_low, mix_weight[layer_index].T, preferred_element_type=jnp.float32
        )
        gelu_value, pullback = jax.vjp(gelu_tanh, conv_out)
        conv_low = pullback(act_grad)[0].astype(jnp.bfloat16)
        padded_wide = stored.astype(jnp.float32)
        grad_padded = grad_halo(conv_low, dilation).astype(jnp.float32)
        conv_wide = grad_padded[dilation : dilation + length]
        kernel_parts[layer_index] = jnp.stack(
            [
                jnp.sum(conv_wide * padded_wide[:length], axis=0),
                jnp.sum(conv_wide * padded_wide[dilation : dilation + length], axis=0),
                jnp.sum(conv_wide * padded_wide[2 * dilation :], axis=0),
            ]
        )
        kernel_wide = kernels[layer_index].astype(jnp.float32)
        norm_grad = (
            kernel_wide[0] * grad_padded[2 * dilation :]
            + kernel_wide[1] * conv_wide
            + kernel_wide[2] * grad_padded[:length]
        )
        upstream = upstream + inv_rms * (
            norm_grad - normed * jnp.mean(norm_grad * normed, axis=-1, keepdims=True)
        )
    embed_part = jnp.dot(
        vocab_hits.astype(jnp.float32).T, upstream, precision=lax.Precision.HIGHEST
    )
    groups = lax.axis_size("dp")
    channels = stream.shape[1]
    tissues, width = tissue_part.shape
    rows = channels // groups
    lanes = 128
    tissue_cells = (
        tissue_part.reshape(tissues, groups, width // groups)
        .transpose(1, 0, 2)
        .reshape(groups, -1)
    )
    tissue_cols = -(-tissue_cells.shape[1] // rows)
    tissue_cells = jnp.pad(
        tissue_cells, ((0, 0), (0, tissue_cols * rows - tissue_cells.shape[1]))
    ).reshape(channels, tissue_cols)
    kernel_local = jnp.stack(kernel_parts).reshape(-1, channels).T
    small = jnp.concatenate([kernel_local, embed_part.T, tissue_cells], axis=1)
    small_widths = [kernel_local.shape[1], embed_part.shape[0], tissue_cols]
    big = [mix_parts[0], mix_parts[1], donor_part, accept_part]
    big_total = sum(piece.shape[1] for piece in big)
    total = -(-(big_total + small.shape[1]) // (2 * lanes)) * (2 * lanes)
    packed = jnp.concatenate(
        [piece.astype(jnp.bfloat16) for piece in big]
        + [
            jnp.pad(small, ((0, 0), (0, total - big_total - small.shape[1]))).astype(
                jnp.bfloat16
            )
        ],
        axis=1,
    )
    half = total // 2
    core = lax.axis_index("seq") % 2
    own = lax.dynamic_slice_in_dim(packed, core * half, half, axis=1)
    other = lax.dynamic_slice_in_dim(packed, (1 - core) * half, half, axis=1)
    partner = lax.ppermute(other, "seq", [(i, i ^ 1) for i in range(count)])
    pair_sum = (own.astype(jnp.float32) + partner.astype(jnp.float32)).astype(jnp.bfloat16)
    scattered = lax.psum_scatter(pair_sum, "dp", scatter_dimension=0, tiled=True)
    share = rows // count
    blocks = scattered.reshape(count, share * half)
    exchanged = lax.all_to_all(blocks, "seq", split_axis=0, concat_axis=0, tiled=True)
    by_core = exchanged.astype(jnp.float32).reshape(count // 2, 2, share * half)
    own_sum = jnp.sum(by_core, axis=0).astype(jnp.bfloat16)
    gathered = lax.all_to_all(
        jnp.broadcast_to(own_sum.reshape(1, -1), (count, own_sum.size)),
        "seq",
        split_axis=0,
        concat_axis=0,
        tiled=True,
    ).reshape((count,) + own_sum.shape)
    summed = jnp.concatenate(
        [gathered[:, 0].reshape(rows, half), gathered[:, 1].reshape(rows, half)], axis=1
    ).astype(jnp.float32)
    mix_grad = summed[:, : 2 * channels].reshape(rows, 2, channels).transpose(1, 0, 2)
    proj_width = donor_part.shape[1]
    donor_grad = summed[:, 2 * channels : 2 * channels + proj_width]
    accept_grad = summed[:, 2 * channels + proj_width : big_total]
    k0 = big_total
    k1 = k0 + small_widths[0]
    k2 = k1 + small_widths[1]
    k3 = k2 + small_widths[2]
    kernel_grad = summed[:, k0:k1].T.reshape(2, 3, rows)
    embed_grad = summed[:, k1:k2].T
    tissue_grad = (
        summed[:, k2:k3].reshape(-1)[: tissues * (width // groups)].reshape(tissues, width // groups)
    )
    features = stream[None]
    input_grad = upstream.astype(jnp.bfloat16)[None]
    return (
        features,
        input_grad,
        mix_grad,
        kernel_grad,
        embed_grad,
        donor_grad,
        accept_grad,
        tissue_grad,
    )


def solution(mesh):
    placed = (
        P("dp", "seq"),
        P(),
        P(),
        P(),
        P(),
        P(),
        P(),
        P("dp", "seq", None),
        P("dp", "seq"),
        P("dp", "seq"),
        P("dp", "seq"),
        P("dp", "seq"),
    )
    return jax.shard_map(
        per_device,
        mesh=mesh,
        in_specs=placed,
        out_specs=(
            P("dp", "seq", None),
            P("dp", "seq", None),
            P(None, "dp", None),
            P(None, None, "dp"),
            P(None, "dp"),
            P("dp", None),
            P("dp", None),
            P(None, "dp"),
        ),
        check_vma=False,
    )
```

```python
import jax
import jax.numpy as jnp
from jax import lax
from jax.sharding import PartitionSpec as P

FIRST_DILATION = 16
SECOND_DILATION = 128


epsilon = 1e-06


def padded(cells, sides, width):
    for axis, dim in sides:
        count = lax.axis_size(axis)
        ends = count - 1
        head = lax.slice_in_dim(cells, 0, width, axis=dim)
        tail = lax.slice_in_dim(cells, cells.shape[dim] - width, cells.shape[dim], axis=dim)
        cells = jnp.concatenate(
            [
                lax.ppermute(tail, axis, [(i, (i + 1) % count) for i in range(ends)]),
                cells,
                lax.ppermute(head, axis, [((i + 1) % count, i) for i in range(ends)]),
            ],
            axis=dim,
        )
    return cells


def normalize(stream_wide):
    inv_rms = lax.rsqrt(jnp.mean(stream_wide * stream_wide, axis=-1, keepdims=True) + epsilon)
    return (stream_wide * inv_rms, inv_rms)


def gelu_tanh(values):
    return jax.nn.gelu(values, approximate=True)


def norm_halo(norm_low, dilation):
    return padded(norm_low, (("seq", 0),), dilation)


def grad_halo(conv_low, dilation):
    return padded(conv_low, (("seq", 0),), dilation)


def per_device(
    tokens,
    embed_table,
    mix_weight,
    kernels,
    donor_proj,
    acceptor_proj,
    tissue_scale,
    junction_dest,
    donor_offset,
    acceptor_offset,
    tissue_ids,
    targets,
):
    length = tokens.shape[1]
    tok_row = tokens[0]
    vocab_hits = tok_row[:, None] == jnp.arange(embed_table.shape[0], dtype=jnp.int32)[None, :]
    stream = jnp.dot(
        vocab_hits.astype(jnp.bfloat16), embed_table, preferred_element_type=jnp.float32
    ).astype(jnp.bfloat16)
    dilation_sizes = (FIRST_DILATION, SECOND_DILATION)
    saved = []
    for layer_index in range(2):
        dilation = dilation_sizes[layer_index]
        stream_wide = stream.astype(jnp.float32)
        normed, inv_rms = normalize(stream_wide)
        norm_low = normed.astype(jnp.bfloat16)
        padded_input = norm_halo(norm_low, dilation)
        padded_wide = padded_input.astype(jnp.float32)
        kernel_wide = kernels[layer_index].astype(jnp.float32)
        conv_out = (
            kernel_wide[0] * padded_wide[:length]
            + kernel_wide[1] * padded_wide[dilation : dilation + length]
            + kernel_wide[2] * padded_wide[2 * dilation :]
        )
        activated = gelu_tanh(conv_out).astype(jnp.bfloat16)
        updated_params = stream_wide + jnp.dot(
            activated, mix_weight[layer_index], preferred_element_type=jnp.float32
        )
        saved.append((normed, inv_rms, padded_input, conv_out, activated))
        stream = updated_params.astype(jnp.bfloat16)
    dest = junction_dest[0, :, 0]
    donor_rows = donor_offset[0]
    accept_rows = acceptor_offset[0]
    tissue_row = tissue_ids[0]
    count = lax.axis_size("seq")
    capacity = 2 * dest.shape[0] // count
    dest_hits = (dest[:, None] == jnp.arange(count, dtype=jnp.int32)[None, :]).astype(jnp.int32)
    before = jnp.cumsum(dest_hits, axis=0) - dest_hits
    slot = jnp.sum(before * dest_hits, axis=1)
    key = dest * capacity + slot
    key_hits = key[:, None] == jnp.arange(count * capacity, dtype=jnp.int32)[None, :]
    request = (
        jnp.sum(jnp.where(key_hits, accept_rows[:, None] + 1, 0), axis=0) - 1
    ).reshape(count, capacity)
    asked = lax.all_to_all(request, "seq", split_axis=0, concat_axis=0, tiled=True)
    valid = (asked >= 0).reshape(-1)
    asked_rows = jnp.where(valid, asked.reshape(-1), 0)
    accepted = stream[asked_rows]
    accept_emb = jnp.dot(accepted, acceptor_proj, preferred_element_type=jnp.float32)
    answer = (
        jnp.where(valid[:, None], accept_emb, 0.0).astype(jnp.bfloat16).reshape(count, capacity, -1)
    )
    returned = lax.all_to_all(answer, "seq", split_axis=0, concat_axis=0, tiled=True)
    key_low = key_hits.astype(jnp.bfloat16)
    accept_wide = jnp.dot(
        key_low, returned.reshape(count * capacity, -1), preferred_element_type=jnp.float32
    )
    donors = stream[donor_rows]
    donor_emb = jnp.dot(donors, donor_proj, preferred_element_type=jnp.float32)
    tissue_hits = (
        tissue_row[:, None] == jnp.arange(tissue_scale.shape[0], dtype=jnp.int32)[None, :]
    ).astype(jnp.float32)
    tissue_rows = jnp.dot(tissue_hits, tissue_scale, precision=lax.Precision.HIGHEST)
    score = jnp.sum(donor_emb * accept_wide * tissue_rows, axis=-1)
    misfit = score - targets[0]
    donor_back = (misfit[:, None] * accept_wide * tissue_rows).astype(jnp.bfloat16)
    accept_back = (misfit[:, None] * donor_emb * tissue_rows).astype(jnp.bfloat16)
    tissue_part = jnp.dot(
        tissue_hits.T, misfit[:, None] * donor_emb * accept_wide, precision=lax.Precision.HIGHEST
    )
    donor_part = jnp.dot(donors.T, donor_back, preferred_element_type=jnp.float32)
    back_buffer = (
        jnp.dot(key_low.T, accept_back, preferred_element_type=jnp.float32)
        .astype(jnp.bfloat16)
        .reshape(count, capacity, -1)
    )
    accept_grads = lax.all_to_all(
        back_buffer, "seq", split_axis=0, concat_axis=0, tiled=True
    ).reshape(count * capacity, -1)
    accept_part = jnp.dot(accepted.T, accept_grads, preferred_element_type=jnp.float32)
    positions = jnp.arange(length, dtype=jnp.int32)[None, :]
    donor_hits = (donor_rows[:, None] == positions).astype(jnp.float32)
    asked_hits = ((asked_rows[:, None] == positions) & valid[:, None]).astype(jnp.float32)
    upstream = jnp.dot(
        donor_hits.T,
        jnp.dot(donor_back, donor_proj.T, preferred_element_type=jnp.float32),
        precision=lax.Precision.HIGHEST,
    ) + jnp.dot(
        asked_hits.T,
        jnp.dot(accept_grads, acceptor_proj.T, preferred_element_type=jnp.float32),
        precision=lax.Precision.HIGHEST,
    )
    mix_parts = [None, None]
    kernel_parts = [None, None]
    for layer_index in (1, 0):
        dilation = dilation_sizes[layer_index]
        normed, inv_rms, stored, conv_out, activated = saved[layer_index]
        upstream_low = upstream.astype(jnp.bfloat16)
        mix_parts[layer_index] = jnp.dot(
            activated.T, upstream_low, preferred_element_type=jnp.float32
        )
        act_grad = jnp.dot(
            upstream_low, mix_weight[layer_index].T, preferred_element_type=jnp.float32
        )
        gelu_value, pullback = jax.vjp(gelu_tanh, conv_out)
        conv_low = pullback(act_grad)[0].astype(jnp.bfloat16)
        padded_wide = stored.astype(jnp.float32)
        grad_padded = grad_halo(conv_low, dilation).astype(jnp.float32)
        conv_wide = grad_padded[dilation : dilation + length]
        kernel_parts[layer_index] = jnp.stack(
            [
                jnp.sum(conv_wide * padded_wide[:length], axis=0),
                jnp.sum(conv_wide * padded_wide[dilation : dilation + length], axis=0),
                jnp.sum(conv_wide * padded_wide[2 * dilation :], axis=0),
            ]
        )
        kernel_wide = kernels[layer_index].astype(jnp.float32)
        norm_grad = (
            kernel_wide[0] * grad_padded[2 * dilation :]
            + kernel_wide[1] * conv_wide
            + kernel_wide[2] * grad_padded[:length]
        )
        upstream = upstream + inv_rms * (
            norm_grad - normed * jnp.mean(norm_grad * normed, axis=-1, keepdims=True)
        )
    embed_part = jnp.dot(
        vocab_hits.astype(jnp.float32).T, upstream, precision=lax.Precision.HIGHEST
    )
    groups = lax.axis_size("dp")
    channels = stream.shape[1]
    tissues, width = tissue_part.shape
    rows = channels // groups
    lanes = 128
    tissue_cells = (
        tissue_part.reshape(tissues, groups, width // groups)
        .transpose(1, 0, 2)
        .reshape(groups, -1)
    )
    tissue_cols = -(-tissue_cells.shape[1] // rows)
    tissue_cells = jnp.pad(
        tissue_cells, ((0, 0), (0, tissue_cols * rows - tissue_cells.shape[1]))
    ).reshape(channels, tissue_cols)
    kernel_local = jnp.stack(kernel_parts).reshape(-1, channels).T
    small = jnp.concatenate([kernel_local, embed_part.T, tissue_cells], axis=1)
    small_widths = [kernel_local.shape[1], embed_part.shape[0], tissue_cols]
    big = [mix_parts[0], mix_parts[1], donor_part, accept_part]
    big_total = sum(piece.shape[1] for piece in big)
    total = -(-(big_total + small.shape[1]) // (2 * lanes)) * (2 * lanes)
    packed = jnp.concatenate(
        [piece.astype(jnp.bfloat16) for piece in big]
        + [
            jnp.pad(small, ((0, 0), (0, total - big_total - small.shape[1]))).astype(
                jnp.bfloat16
            )
        ],
        axis=1,
    )
    half = total // 2
    core = lax.axis_index("seq") % 2
    own = lax.dynamic_slice_in_dim(packed, core * half, half, axis=1)
    other = lax.dynamic_slice_in_dim(packed, (1 - core) * half, half, axis=1)
    partner = lax.ppermute(other, "seq", [(i, i ^ 1) for i in range(count)])
    pair_sum = (own.astype(jnp.float32) + partner.astype(jnp.float32)).astype(jnp.bfloat16)
    scattered = lax.psum_scatter(pair_sum, "dp", scatter_dimension=0, tiled=True)
    share = rows // count
    tiles = share * half // lanes
    blocks = scattered.reshape(count, tiles, lanes)
    exchanged = lax.all_to_all(blocks, "seq", split_axis=0, concat_axis=0, tiled=True)
    by_core = exchanged.astype(jnp.float32).reshape(count // 2, 2, tiles, lanes)
    own_sum = jnp.sum(by_core, axis=0).astype(jnp.bfloat16).reshape(2 * tiles, lanes)
    gathered = lax.all_gather(own_sum, "seq", axis=0, tiled=False).reshape(
        count, 2, share * half
    )
    summed = jnp.concatenate(
        [gathered[:, 0].reshape(rows, half), gathered[:, 1].reshape(rows, half)], axis=1
    ).astype(jnp.float32)
    mix_grad = summed[:, : 2 * channels].reshape(rows, 2, channels).transpose(1, 0, 2)
    proj_width = donor_part.shape[1]
    donor_grad = summed[:, 2 * channels : 2 * channels + proj_width]
    accept_grad = summed[:, 2 * channels + proj_width : big_total]
    k0 = big_total
    k1 = k0 + small_widths[0]
    k2 = k1 + small_widths[1]
    k3 = k2 + small_widths[2]
    kernel_grad = summed[:, k0:k1].T.reshape(2, 3, rows)
    embed_grad = summed[:, k1:k2].T
    tissue_grad = (
        summed[:, k2:k3].reshape(-1)[: tissues * (width // groups)].reshape(tissues, width // groups)
    )
    features = stream[None]
    input_grad = upstream.astype(jnp.bfloat16)[None]
    return (
        features,
        input_grad,
        mix_grad,
        kernel_grad,
        embed_grad,
        donor_grad,
        accept_grad,
        tissue_grad,
    )


def solution(mesh):
    placed = (
        P("dp", "seq"),
        P(),
        P(),
        P(),
        P(),
        P(),
        P(),
        P("dp", "seq", None),
        P("dp", "seq"),
        P("dp", "seq"),
        P("dp", "seq"),
        P("dp", "seq"),
    )
    return jax.shard_map(
        per_device,
        mesh=mesh,
        in_specs=placed,
        out_specs=(
            P("dp", "seq", None),
            P("dp", "seq", None),
            P(None, "dp", None),
            P(None, None, "dp"),
            P(None, "dp"),
            P("dp", None),
            P("dp", None),
            P(None, "dp"),
        ),
        check_vma=False,
    )
```

```python
import jax
import jax.numpy as jnp
from jax import lax
from jax.sharding import PartitionSpec as P

FIRST_DILATION = 16
SECOND_DILATION = 128


epsilon = 1e-06


def padded(cells, sides, width):
    for axis, dim in sides:
        count = lax.axis_size(axis)
        ends = count - 1
        head = lax.slice_in_dim(cells, 0, width, axis=dim)
        tail = lax.slice_in_dim(cells, cells.shape[dim] - width, cells.shape[dim], axis=dim)
        cells = jnp.concatenate(
            [
                lax.ppermute(tail, axis, [(i, (i + 1) % count) for i in range(ends)]),
                cells,
                lax.ppermute(head, axis, [((i + 1) % count, i) for i in range(ends)]),
            ],
            axis=dim,
        )
    return cells


def normalize(stream_wide):
    inv_rms = lax.rsqrt(jnp.mean(stream_wide * stream_wide, axis=-1, keepdims=True) + epsilon)
    return (stream_wide * inv_rms, inv_rms)


def gelu_tanh(values):
    return jax.nn.gelu(values, approximate=True)


def norm_halo(norm_low, dilation):
    return padded(norm_low, (("seq", 0),), dilation)


def grad_halo(conv_low, dilation):
    return padded(conv_low, (("seq", 0),), dilation)


def per_device(
    tokens,
    embed_table,
    mix_weight,
    kernels,
    donor_proj,
    acceptor_proj,
    tissue_scale,
    junction_dest,
    donor_offset,
    acceptor_offset,
    tissue_ids,
    targets,
):
    length = tokens.shape[1]
    tok_row = tokens[0]
    vocab_hits = tok_row[:, None] == jnp.arange(embed_table.shape[0], dtype=jnp.int32)[None, :]
    stream = jnp.dot(
        vocab_hits.astype(jnp.bfloat16), embed_table, preferred_element_type=jnp.float32
    ).astype(jnp.bfloat16)
    dilation_sizes = (FIRST_DILATION, SECOND_DILATION)
    saved = []
    for layer_index in range(2):
        dilation = dilation_sizes[layer_index]
        stream_wide = stream.astype(jnp.float32)
        normed, inv_rms = normalize(stream_wide)
        norm_low = normed.astype(jnp.bfloat16)
        padded_input = norm_halo(norm_low, dilation)
        padded_wide = padded_input.astype(jnp.float32)
        kernel_wide = kernels[layer_index].astype(jnp.float32)
        conv_out = (
            kernel_wide[0] * padded_wide[:length]
            + kernel_wide[1] * padded_wide[dilation : dilation + length]
            + kernel_wide[2] * padded_wide[2 * dilation :]
        )
        activated = gelu_tanh(conv_out).astype(jnp.bfloat16)
        updated_params = stream_wide + jnp.dot(
            activated, mix_weight[layer_index], preferred_element_type=jnp.float32
        )
        saved.append((normed, inv_rms, padded_input, conv_out, activated))
        stream = updated_params.astype(jnp.bfloat16)
    dest = junction_dest[0, :, 0]
    donor_rows = donor_offset[0]
    accept_rows = acceptor_offset[0]
    tissue_row = tissue_ids[0]
    count = lax.axis_size("seq")
    capacity = 2 * dest.shape[0] // count
    dest_hits = (dest[:, None] == jnp.arange(count, dtype=jnp.int32)[None, :]).astype(jnp.int32)
    before = jnp.cumsum(dest_hits, axis=0) - dest_hits
    slot = jnp.sum(before * dest_hits, axis=1)
    key = dest * capacity + slot
    key_hits = key[:, None] == jnp.arange(count * capacity, dtype=jnp.int32)[None, :]
    request = (
        jnp.sum(jnp.where(key_hits, accept_rows[:, None] + 1, 0), axis=0) - 1
    ).reshape(count, capacity)
    asked = lax.all_to_all(request, "seq", split_axis=0, concat_axis=0, tiled=True)
    valid = (asked >= 0).reshape(-1)
    asked_rows = jnp.where(valid, asked.reshape(-1), 0)
    accepted = stream[asked_rows]
    accept_emb = jnp.dot(accepted, acceptor_proj, preferred_element_type=jnp.float32)
    answer = (
        jnp.where(valid[:, None], accept_emb, 0.0).astype(jnp.bfloat16).reshape(count, capacity, -1)
    )
    returned = lax.all_to_all(answer, "seq", split_axis=0, concat_axis=0, tiled=True)
    key_low = key_hits.astype(jnp.bfloat16)
    accept_wide = jnp.dot(
        key_low, returned.reshape(count * capacity, -1), preferred_element_type=jnp.float32
    )
    donors = stream[donor_rows]
    donor_emb = jnp.dot(donors, donor_proj, preferred_element_type=jnp.float32)
    tissue_hits = (
        tissue_row[:, None] == jnp.arange(tissue_scale.shape[0], dtype=jnp.int32)[None, :]
    ).astype(jnp.float32)
    tissue_rows = jnp.dot(tissue_hits, tissue_scale, precision=lax.Precision.HIGHEST)
    score = jnp.sum(donor_emb * accept_wide * tissue_rows, axis=-1)
    misfit = score - targets[0]
    donor_back = (misfit[:, None] * accept_wide * tissue_rows).astype(jnp.bfloat16)
    accept_back = (misfit[:, None] * donor_emb * tissue_rows).astype(jnp.bfloat16)
    tissue_part = jnp.dot(
        tissue_hits.T, misfit[:, None] * donor_emb * accept_wide, precision=lax.Precision.HIGHEST
    )
    donor_part = jnp.dot(donors.T, donor_back, preferred_element_type=jnp.float32)
    back_buffer = (
        jnp.dot(key_low.T, accept_back, preferred_element_type=jnp.float32)
        .astype(jnp.bfloat16)
        .reshape(count, capacity, -1)
    )
    accept_grads = lax.all_to_all(
        back_buffer, "seq", split_axis=0, concat_axis=0, tiled=True
    ).reshape(count * capacity, -1)
    accept_part = jnp.dot(accepted.T, accept_grads, preferred_element_type=jnp.float32)
    positions = jnp.arange(length, dtype=jnp.int32)[None, :]
    donor_hits = (donor_rows[:, None] == positions).astype(jnp.float32)
    asked_hits = ((asked_rows[:, None] == positions) & valid[:, None]).astype(jnp.float32)
    upstream = jnp.dot(
        donor_hits.T,
        jnp.dot(donor_back, donor_proj.T, preferred_element_type=jnp.float32),
        precision=lax.Precision.HIGHEST,
    ) + jnp.dot(
        asked_hits.T,
        jnp.dot(accept_grads, acceptor_proj.T, preferred_element_type=jnp.float32),
        precision=lax.Precision.HIGHEST,
    )
    mix_parts = [None, None]
    kernel_parts = [None, None]
    for layer_index in (1, 0):
        dilation = dilation_sizes[layer_index]
        normed, inv_rms, stored, conv_out, activated = saved[layer_index]
        upstream_low = upstream.astype(jnp.bfloat16)
        mix_parts[layer_index] = jnp.dot(
            activated.T, upstream_low, preferred_element_type=jnp.float32
        )
        act_grad = jnp.dot(
            upstream_low, mix_weight[layer_index].T, preferred_element_type=jnp.float32
        )
        gelu_value, pullback = jax.vjp(gelu_tanh, conv_out)
        conv_low = pullback(act_grad)[0].astype(jnp.bfloat16)
        padded_wide = stored.astype(jnp.float32)
        grad_padded = grad_halo(conv_low, dilation).astype(jnp.float32)
        conv_wide = grad_padded[dilation : dilation + length]
        kernel_parts[layer_index] = jnp.stack(
            [
                jnp.sum(conv_wide * padded_wide[:length], axis=0),
                jnp.sum(conv_wide * padded_wide[dilation : dilation + length], axis=0),
                jnp.sum(conv_wide * padded_wide[2 * dilation :], axis=0),
            ]
        )
        kernel_wide = kernels[layer_index].astype(jnp.float32)
        norm_grad = (
            kernel_wide[0] * grad_padded[2 * dilation :]
            + kernel_wide[1] * conv_wide
            + kernel_wide[2] * grad_padded[:length]
        )
        upstream = upstream + inv_rms * (
            norm_grad - normed * jnp.mean(norm_grad * normed, axis=-1, keepdims=True)
        )
    embed_part = jnp.dot(
        vocab_hits.astype(jnp.float32).T, upstream, precision=lax.Precision.HIGHEST
    )
    groups = lax.axis_size("dp")
    channels = stream.shape[1]
    tissues, width = tissue_part.shape
    rows = channels // groups
    lanes = 128
    tissue_cells = (
        tissue_part.reshape(tissues, groups, width // groups)
        .transpose(1, 0, 2)
        .reshape(groups, -1)
    )
    tissue_cols = -(-tissue_cells.shape[1] // rows)
    tissue_cells = jnp.pad(
        tissue_cells, ((0, 0), (0, tissue_cols * rows - tissue_cells.shape[1]))
    ).reshape(channels, tissue_cols)
    kernel_local = jnp.stack(kernel_parts).reshape(-1, channels).T
    small = jnp.concatenate([kernel_local, embed_part.T, tissue_cells], axis=1)
    small_widths = [kernel_local.shape[1], embed_part.shape[0], tissue_cols]
    big = [mix_parts[0], mix_parts[1], donor_part, accept_part]
    big_total = sum(piece.shape[1] for piece in big)
    total = -(-(big_total + small.shape[1]) // (2 * lanes)) * (2 * lanes)
    packed = jnp.concatenate(
        [piece.astype(jnp.bfloat16) for piece in big]
        + [
            jnp.pad(small, ((0, 0), (0, total - big_total - small.shape[1]))).astype(
                jnp.bfloat16
            )
        ],
        axis=1,
    )
    half = total // 2
    core = lax.axis_index("seq") % 2
    own = lax.dynamic_slice_in_dim(packed, core * half, half, axis=1)
    other = lax.dynamic_slice_in_dim(packed, (1 - core) * half, half, axis=1)
    partner = lax.ppermute(other, "seq", [(i, i ^ 1) for i in range(count)])
    pair_sum = (own.astype(jnp.float32) + partner.astype(jnp.float32)).astype(jnp.bfloat16)
    scattered = lax.psum_scatter(pair_sum, "dp", scatter_dimension=0, tiled=True)
    share = rows // count
    tiles = share * half // lanes
    blocks = scattered.reshape(count, tiles, lanes)
    exchanged = lax.all_to_all(blocks, "seq", split_axis=0, concat_axis=0, tiled=True)
    by_core = exchanged.astype(jnp.float32).reshape(count // 2, 2, tiles, lanes)
    own_sum = jnp.sum(by_core, axis=0).astype(jnp.bfloat16).reshape(2 * tiles, lanes)
    gathered = lax.all_to_all(
        jnp.broadcast_to(own_sum[None], (count,) + own_sum.shape),
        "seq",
        split_axis=0,
        concat_axis=0,
        tiled=True,
    ).reshape(count, 2, share * half)
    summed = jnp.concatenate(
        [gathered[:, 0].reshape(rows, half), gathered[:, 1].reshape(rows, half)], axis=1
    ).astype(jnp.float32)
    mix_grad = summed[:, : 2 * channels].reshape(rows, 2, channels).transpose(1, 0, 2)
    proj_width = donor_part.shape[1]
    donor_grad = summed[:, 2 * channels : 2 * channels + proj_width]
    accept_grad = summed[:, 2 * channels + proj_width : big_total]
    k0 = big_total
    k1 = k0 + small_widths[0]
    k2 = k1 + small_widths[1]
    k3 = k2 + small_widths[2]
    kernel_grad = summed[:, k0:k1].T.reshape(2, 3, rows)
    embed_grad = summed[:, k1:k2].T
    tissue_grad = (
        summed[:, k2:k3].reshape(-1)[: tissues * (width // groups)].reshape(tissues, width // groups)
    )
    features = stream[None]
    input_grad = upstream.astype(jnp.bfloat16)[None]
    return (
        features,
        input_grad,
        mix_grad,
        kernel_grad,
        embed_grad,
        donor_grad,
        accept_grad,
        tissue_grad,
    )


def solution(mesh):
    placed = (
        P("dp", "seq"),
        P(),
        P(),
        P(),
        P(),
        P(),
        P(),
        P("dp", "seq", None),
        P("dp", "seq"),
        P("dp", "seq"),
        P("dp", "seq"),
        P("dp", "seq"),
    )
    return jax.shard_map(
        per_device,
        mesh=mesh,
        in_specs=placed,
        out_specs=(
            P("dp", "seq", None),
            P("dp", "seq", None),
            P(None, "dp", None),
            P(None, None, "dp"),
            P(None, "dp"),
            P("dp", None),
            P("dp", None),
            P(None, "dp"),
        ),
        check_vma=False,
    )
```

```python
import jax
import jax.numpy as jnp
from jax import lax
from jax.sharding import PartitionSpec as P

FIRST_DILATION = 16
SECOND_DILATION = 128


epsilon = 1e-06


def padded(cells, sides, width):
    for axis, dim in sides:
        count = lax.axis_size(axis)
        ends = count - 1
        head = lax.slice_in_dim(cells, 0, width, axis=dim)
        tail = lax.slice_in_dim(cells, cells.shape[dim] - width, cells.shape[dim], axis=dim)
        cells = jnp.concatenate(
            [
                lax.ppermute(tail, axis, [(i, (i + 1) % count) for i in range(ends)]),
                cells,
                lax.ppermute(head, axis, [((i + 1) % count, i) for i in range(ends)]),
            ],
            axis=dim,
        )
    return cells


def normalize(stream_wide):
    inv_rms = lax.rsqrt(jnp.mean(stream_wide * stream_wide, axis=-1, keepdims=True) + epsilon)
    return (stream_wide * inv_rms, inv_rms)


def gelu_tanh(values):
    return jax.nn.gelu(values, approximate=True)


def norm_halo(norm_low, dilation):
    return padded(norm_low, (("seq", 0),), dilation)


def grad_halo(conv_low, dilation):
    return padded(conv_low, (("seq", 0),), dilation)


def per_device(
    tokens,
    embed_table,
    mix_weight,
    kernels,
    donor_proj,
    acceptor_proj,
    tissue_scale,
    junction_dest,
    donor_offset,
    acceptor_offset,
    tissue_ids,
    targets,
):
    length = tokens.shape[1]
    tok_row = tokens[0]
    vocab = jnp.arange(embed_table.shape[0], dtype=jnp.int32)[None, :]
    vocab_hits = tok_row[:, None] == vocab
    first = FIRST_DILATION
    tok_wide = padded(tok_row, (("seq", 0),), first)
    wide_stream = jnp.dot(
        (tok_wide[:, None] == vocab).astype(jnp.bfloat16),
        embed_table,
        preferred_element_type=jnp.float32,
    ).astype(jnp.bfloat16)
    stream = wide_stream[first : first + length]
    place = lax.axis_index("seq")
    spots = jnp.arange(length + 2 * first, dtype=jnp.int32)
    inside = ((spots >= first) | (place > 0)) & (
        (spots < first + length) | (place < lax.axis_size("seq") - 1)
    )
    dilation_sizes = (FIRST_DILATION, SECOND_DILATION)
    saved = []
    for layer_index in range(2):
        dilation = dilation_sizes[layer_index]
        stream_wide = stream.astype(jnp.float32)
        if layer_index == 0:
            normed_all, inv_all = normalize(wide_stream.astype(jnp.float32))
            normed = normed_all[first : first + length]
            inv_rms = inv_all[first : first + length]
            padded_input = jnp.where(inside[:, None], normed_all.astype(jnp.bfloat16), 0)
        else:
            normed, inv_rms = normalize(stream_wide)
            norm_low = normed.astype(jnp.bfloat16)
            padded_input = norm_halo(norm_low, dilation)
        padded_wide = padded_input.astype(jnp.float32)
        kernel_wide = kernels[layer_index].astype(jnp.float32)
        conv_out = (
            kernel_wide[0] * padded_wide[:length]
            + kernel_wide[1] * padded_wide[dilation : dilation + length]
            + kernel_wide[2] * padded_wide[2 * dilation :]
        )
        activated = gelu_tanh(conv_out).astype(jnp.bfloat16)
        updated_params = stream_wide + jnp.dot(
            activated, mix_weight[layer_index], preferred_element_type=jnp.float32
        )
        saved.append((normed, inv_rms, padded_input, conv_out, activated))
        stream = updated_params.astype(jnp.bfloat16)
    dest = junction_dest[0, :, 0]
    donor_rows = donor_offset[0]
    accept_rows = acceptor_offset[0]
    tissue_row = tissue_ids[0]
    count = lax.axis_size("seq")
    capacity = 2 * dest.shape[0] // count
    dest_hits = (dest[:, None] == jnp.arange(count, dtype=jnp.int32)[None, :]).astype(jnp.int32)
    before = jnp.cumsum(dest_hits, axis=0) - dest_hits
    slot = jnp.sum(before * dest_hits, axis=1)
    key = dest * capacity + slot
    key_hits = key[:, None] == jnp.arange(count * capacity, dtype=jnp.int32)[None, :]
    request = (
        jnp.sum(jnp.where(key_hits, accept_rows[:, None] + 1, 0), axis=0) - 1
    ).reshape(count, capacity)
    asked = lax.all_to_all(request, "seq", split_axis=0, concat_axis=0, tiled=True)
    valid = (asked >= 0).reshape(-1)
    asked_rows = jnp.where(valid, asked.reshape(-1), 0)
    accepted = stream[asked_rows]
    accept_emb = jnp.dot(accepted, acceptor_proj, preferred_element_type=jnp.float32)
    answer = (
        jnp.where(valid[:, None], accept_emb, 0.0).astype(jnp.bfloat16).reshape(count, capacity, -1)
    )
    returned = lax.all_to_all(answer, "seq", split_axis=0, concat_axis=0, tiled=True)
    key_low = key_hits.astype(jnp.bfloat16)
    accept_wide = jnp.dot(
        key_low, returned.reshape(count * capacity, -1), preferred_element_type=jnp.float32
    )
    donors = stream[donor_rows]
    donor_emb = jnp.dot(donors, donor_proj, preferred_element_type=jnp.float32)
    tissue_hits = (
        tissue_row[:, None] == jnp.arange(tissue_scale.shape[0], dtype=jnp.int32)[None, :]
    ).astype(jnp.float32)
    tissue_rows = jnp.dot(tissue_hits, tissue_scale, precision=lax.Precision.HIGHEST)
    score = jnp.sum(donor_emb * accept_wide * tissue_rows, axis=-1)
    misfit = score - targets[0]
    donor_back = (misfit[:, None] * accept_wide * tissue_rows).astype(jnp.bfloat16)
    accept_back = (misfit[:, None] * donor_emb * tissue_rows).astype(jnp.bfloat16)
    tissue_part = jnp.dot(
        tissue_hits.T, misfit[:, None] * donor_emb * accept_wide, precision=lax.Precision.HIGHEST
    )
    donor_part = jnp.dot(donors.T, donor_back, preferred_element_type=jnp.float32)
    back_buffer = (
        jnp.dot(key_low.T, accept_back, preferred_element_type=jnp.float32)
        .astype(jnp.bfloat16)
        .reshape(count, capacity, -1)
    )
    accept_grads = lax.all_to_all(
        back_buffer, "seq", split_axis=0, concat_axis=0, tiled=True
    ).reshape(count * capacity, -1)
    accept_part = jnp.dot(accepted.T, accept_grads, preferred_element_type=jnp.float32)
    positions = jnp.arange(length, dtype=jnp.int32)[None, :]
    donor_hits = (donor_rows[:, None] == positions).astype(jnp.float32)
    asked_hits = ((asked_rows[:, None] == positions) & valid[:, None]).astype(jnp.float32)
    upstream = jnp.dot(
        donor_hits.T,
        jnp.dot(donor_back, donor_proj.T, preferred_element_type=jnp.float32),
        precision=lax.Precision.HIGHEST,
    ) + jnp.dot(
        asked_hits.T,
        jnp.dot(accept_grads, acceptor_proj.T, preferred_element_type=jnp.float32),
        precision=lax.Precision.HIGHEST,
    )
    mix_parts = [None, None]
    kernel_parts = [None, None]
    for layer_index in (1, 0):
        dilation = dilation_sizes[layer_index]
        normed, inv_rms, stored, conv_out, activated = saved[layer_index]
        upstream_low = upstream.astype(jnp.bfloat16)
        mix_parts[layer_index] = jnp.dot(
            activated.T, upstream_low, preferred_element_type=jnp.float32
        )
        act_grad = jnp.dot(
            upstream_low, mix_weight[layer_index].T, preferred_element_type=jnp.float32
        )
        gelu_value, pullback = jax.vjp(gelu_tanh, conv_out)
        conv_low = pullback(act_grad)[0].astype(jnp.bfloat16)
        padded_wide = stored.astype(jnp.float32)
        grad_padded = grad_halo(conv_low, dilation).astype(jnp.float32)
        conv_wide = grad_padded[dilation : dilation + length]
        kernel_parts[layer_index] = jnp.stack(
            [
                jnp.sum(conv_wide * padded_wide[:length], axis=0),
                jnp.sum(conv_wide * padded_wide[dilation : dilation + length], axis=0),
                jnp.sum(conv_wide * padded_wide[2 * dilation :], axis=0),
            ]
        )
        kernel_wide = kernels[layer_index].astype(jnp.float32)
        norm_grad = (
            kernel_wide[0] * grad_padded[2 * dilation :]
            + kernel_wide[1] * conv_wide
            + kernel_wide[2] * grad_padded[:length]
        )
        upstream = upstream + inv_rms * (
            norm_grad - normed * jnp.mean(norm_grad * normed, axis=-1, keepdims=True)
        )
    embed_part = jnp.dot(
        vocab_hits.astype(jnp.float32).T, upstream, precision=lax.Precision.HIGHEST
    )
    groups = lax.axis_size("dp")
    channels = stream.shape[1]
    tissues, width = tissue_part.shape
    rows = channels // groups
    lanes = 128
    tissue_cells = (
        tissue_part.reshape(tissues, groups, width // groups)
        .transpose(1, 0, 2)
        .reshape(groups, -1)
    )
    tissue_cols = -(-tissue_cells.shape[1] // rows)
    tissue_cells = jnp.pad(
        tissue_cells, ((0, 0), (0, tissue_cols * rows - tissue_cells.shape[1]))
    ).reshape(channels, tissue_cols)
    kernel_local = jnp.stack(kernel_parts).reshape(-1, channels).T
    small = jnp.concatenate([kernel_local, embed_part.T, tissue_cells], axis=1)
    small_widths = [kernel_local.shape[1], embed_part.shape[0], tissue_cols]
    big = [mix_parts[0], mix_parts[1], donor_part, accept_part]
    big_total = sum(piece.shape[1] for piece in big)
    total = -(-(big_total + small.shape[1]) // (2 * lanes)) * (2 * lanes)
    packed = jnp.concatenate(
        [piece.astype(jnp.bfloat16) for piece in big]
        + [
            jnp.pad(small, ((0, 0), (0, total - big_total - small.shape[1]))).astype(
                jnp.bfloat16
            )
        ],
        axis=1,
    )
    half = total // 2
    core = lax.axis_index("seq") % 2
    own = lax.dynamic_slice_in_dim(packed, core * half, half, axis=1)
    other = lax.dynamic_slice_in_dim(packed, (1 - core) * half, half, axis=1)
    partner = lax.ppermute(other, "seq", [(i, i ^ 1) for i in range(count)])
    pair_sum = (own.astype(jnp.float32) + partner.astype(jnp.float32)).astype(jnp.bfloat16)
    scattered = lax.psum_scatter(pair_sum, "dp", scatter_dimension=0, tiled=True)
    share = rows // count
    tiles = share * half // lanes
    blocks = scattered.reshape(count, tiles, lanes)
    exchanged = lax.all_to_all(blocks, "seq", split_axis=0, concat_axis=0, tiled=True)
    by_core = exchanged.astype(jnp.float32).reshape(count // 2, 2, tiles, lanes)
    own_sum = jnp.sum(by_core, axis=0).astype(jnp.bfloat16).reshape(2 * tiles, lanes)
    gathered = lax.all_to_all(
        jnp.broadcast_to(own_sum[None], (count,) + own_sum.shape),
        "seq",
        split_axis=0,
        concat_axis=0,
        tiled=True,
    ).reshape(count, 2, share * half)
    summed = jnp.concatenate(
        [gathered[:, 0].reshape(rows, half), gathered[:, 1].reshape(rows, half)], axis=1
    ).astype(jnp.float32)
    mix_grad = summed[:, : 2 * channels].reshape(rows, 2, channels).transpose(1, 0, 2)
    proj_width = donor_part.shape[1]
    donor_grad = summed[:, 2 * channels : 2 * channels + proj_width]
    accept_grad = summed[:, 2 * channels + proj_width : big_total]
    k0 = big_total
    k1 = k0 + small_widths[0]
    k2 = k1 + small_widths[1]
    k3 = k2 + small_widths[2]
    kernel_grad = summed[:, k0:k1].T.reshape(2, 3, rows)
    embed_grad = summed[:, k1:k2].T
    tissue_grad = (
        summed[:, k2:k3].reshape(-1)[: tissues * (width // groups)].reshape(tissues, width // groups)
    )
    features = stream[None]
    input_grad = upstream.astype(jnp.bfloat16)[None]
    return (
        features,
        input_grad,
        mix_grad,
        kernel_grad,
        embed_grad,
        donor_grad,
        accept_grad,
        tissue_grad,
    )


def solution(mesh):
    placed = (
        P("dp", "seq"),
        P(),
        P(),
        P(),
        P(),
        P(),
        P(),
        P("dp", "seq", None),
        P("dp", "seq"),
        P("dp", "seq"),
        P("dp", "seq"),
        P("dp", "seq"),
    )
    return jax.shard_map(
        per_device,
        mesh=mesh,
        in_specs=placed,
        out_specs=(
            P("dp", "seq", None),
            P("dp", "seq", None),
            P(None, "dp", None),
            P(None, None, "dp"),
            P(None, "dp"),
            P("dp", None),
            P("dp", None),
            P(None, "dp"),
        ),
        check_vma=False,
    )
```
